1024 devices in a mesh: dp: 4 (over z_lo), seq: 256 (over x, z_hi, y, core).
Axes of the slice: x: 8, y: 8, z: 8 (z_hi: 2, z_lo: 4; z = z_hi * 4 + z_lo), core: 2. Of those that a mesh axis runs over, the one named last changes fastest.
Arguments:
- grad_out: bfloat16 [4, 32768, 6144], P('dp', 'seq'), may hold values from -0.00390625 to 0.00390625
- w_out: bfloat16 [128, 6144], P(None, 'dp'), may hold values from -0.078125 to 0.078125
- queries: bfloat16 [4, 32768, 128], P('dp', 'seq'), may hold values from -6 to 6
- keys_in: bfloat16 [4, 32768, 128], P('dp', 'seq'), may hold values from -6 to 6
- values: bfloat16 [4, 32768, 128], P('dp', 'seq'), may hold values from -6 to 6
- log_decay: float32 [4, 2, 32768], P('dp', None, 'seq'), may hold values from -1.2 to 0
- kv_state: bfloat16 [4, 256, 2, 64, 64], P('dp', 'seq'), may hold values from -512 to 512
Outputs:
- grad_q: bfloat16 [4, 32768, 128], P('dp', 'seq')
- grad_k: bfloat16 [4, 32768, 128], P('dp', 'seq')
- grad_v: bfloat16 [4, 32768, 128], P('dp', 'seq')
The draws below stay inside these ranges and needn't reach their ends.
All inputs are finite; a program needn't handle non-finite values.
Results may differ from the reference program's by a relative error of at most 0.0059.
Values may be sent and summed in bfloat16 or wider, within the bound.
No kernel may reach another device: no remote copies, remote signals or barrier semaphores. Data moves between devices by JAX's collectives and lax.ppermute only.
A program may use at most 64 MiB of HBM per device.

```python
import math
import jax
import jax.numpy as jnp
from jax import lax

D = 6144
DH = 64
FEW_HEADS_SHARE = 2
TOK_DEV = 128
HD = 128
NCH = 256
SPAN_OF_STEPS = 32768
STREAMS_IN_STEP = 4


def draw_log_decay(key, part):
    keylist = jax.random.split(key, 6)
    dims_head = (STREAMS_IN_STEP, FEW_HEADS_SHARE, 1)
    fast_share = 0.5
    slow_rate = jnp.exp(jax.random.uniform(keylist[1], dims_head, jnp.float32, math.log(0.05), math.log(0.4))) / SPAN_OF_STEPS
    fast_rate = 1.0 / jax.random.uniform(keylist[2], dims_head, jnp.float32, 30.0, 50.0)
    chosen = jax.random.uniform(keylist[0], dims_head, jnp.float32) < fast_share
    forgetting_rate = jnp.where(chosen, fast_rate, slow_rate)
    scaling_coefficient = jnp.exp(jax.random.uniform(keylist[3], (STREAMS_IN_STEP, FEW_HEADS_SHARE, NCH), jnp.float32, math.log(0.5), math.log(2.0)))
    scaling_coefficient = jnp.repeat(scaling_coefficient, TOK_DEV, axis=2)
    index_entries = jax.random.randint(keylist[4], (STREAMS_IN_STEP, FEW_HEADS_SHARE, 2), 0, SPAN_OF_STEPS)
    objective_scores = jax.random.uniform(keylist[5], (STREAMS_IN_STEP, FEW_HEADS_SHARE, 2), jnp.float32, 0.2, 0.4)
    word_index = lax.broadcasted_iota(jnp.int32, (STREAMS_IN_STEP, FEW_HEADS_SHARE, SPAN_OF_STEPS), 2)
    clustered_spans = jnp.zeros((STREAMS_IN_STEP, FEW_HEADS_SHARE, SPAN_OF_STEPS), jnp.float32)
    for overall_number in range(2):
        clustered_spans = clustered_spans + jnp.where(word_index == index_entries[:, :, overall_number:overall_number + 1], jnp.log(1.0 - objective_scores[:, :, overall_number:overall_number + 1]), 0.0)
    return -forgetting_rate * scaling_coefficient + clustered_spans


def block_scale(stream_key, extent, pieces, low, top_value):
    def one(axis_at, blocks):
        steps = jax.random.uniform(jax.random.fold_in(jax.random.fold_in(stream_key, 6), axis_at), (blocks,), jnp.float32, low / len(pieces), top_value / len(pieces))
        return jnp.repeat(jnp.exp(steps), extent[axis_at] // blocks).reshape((-1,) + (1,) * (len(extent) - axis_at - 1))

    loudness = one(*pieces[0])
    for cut in pieces[1:]:
        loudness = loudness * one(*cut)
    return loudness


def bell_draw(stream_key, dims, scale, bound, shards=(), kind=jnp.bfloat16):
    array = scale * jax.random.normal(stream_key, dims, jnp.float32)
    if shards:
        array = array * block_scale(stream_key, dims, shards, -0.22, 0.18)
    return jnp.clip(array, -bound, bound).astype(kind)


def setup_inputs(seed: int = 0) -> dict:
    keys = jax.random.split(jax.random.key(seed), 8)
    grad_out = bell_draw(keys[0], (STREAMS_IN_STEP, SPAN_OF_STEPS, D), ((DH * SPAN_OF_STEPS) ** -0.5), 0.00390625, ((0, 4), (1, 256)))
    w_out = bell_draw(keys[1], (HD, D), D ** -0.5, 0.078125, ((1, 4),))
    queries = bell_draw(keys[2], (STREAMS_IN_STEP, SPAN_OF_STEPS, HD), 1.0, 6.0, ((0, 4), (1, 256)))
    keys_in = bell_draw(keys[3], (STREAMS_IN_STEP, SPAN_OF_STEPS, HD), 1.0, 6.0, ((0, 4), (1, 256)))
    values = bell_draw(keys[4], (STREAMS_IN_STEP, SPAN_OF_STEPS, HD), 1.0, 6.0, ((0, 4), (1, 256)))
    log_decay = draw_log_decay(jax.random.fold_in(keys[7], 71), 0)
    kv_state = bell_draw(keys[6], (STREAMS_IN_STEP, NCH, FEW_HEADS_SHARE, DH, DH), ((SPAN_OF_STEPS // 4) ** 0.5), 512.0, ((0, 4), (1, 256)))
    return dict(grad_out=grad_out, w_out=w_out, queries=queries, keys_in=keys_in, values=values, log_decay=log_decay, kv_state=kv_state)


def reference(grad_out, w_out, queries, keys_in, values, log_decay, kv_state):
    def one_sequence(packed):
        grad_rows, query_rows, key_rows, value_rows, decay_rows, saved_state = packed
        projected = jnp.dot(grad_rows, w_out.T, preferred_element_type=jnp.float32).astype(jnp.bfloat16)
        grad_attn = projected.reshape(NCH, TOK_DEV, FEW_HEADS_SHARE, DH).astype(jnp.float32)
        query_f = query_rows.reshape(NCH, TOK_DEV, FEW_HEADS_SHARE, DH).astype(jnp.float32)
        key_f = key_rows.reshape(NCH, TOK_DEV, FEW_HEADS_SHARE, DH).astype(jnp.float32)
        value_f = value_rows.reshape(NCH, TOK_DEV, FEW_HEADS_SHARE, DH).astype(jnp.float32)
        cumul = jnp.cumsum(decay_rows.reshape(FEW_HEADS_SHARE, NCH, TOK_DEV), axis=2).transpose(1, 0, 2)
        growth = jnp.exp(cumul).transpose(0, 2, 1)[..., None]
        scaled_q = lax.optimization_barrier((query_f * growth).astype(jnp.bfloat16)).astype(jnp.float32)
        block_terms = jnp.einsum("nthd,nthe->nhde", scaled_q, grad_attn)
        block_decay = jnp.exp(cumul[:, :, -1])

        def backward_step(carried, item):
            terms, decay = item
            return terms + decay[:, None, None] * carried, carried

        _, future = lax.scan(backward_step, jnp.zeros((FEW_HEADS_SHARE, DH, DH), jnp.float32), (block_terms, block_decay), reverse=True)
        future_f = lax.optimization_barrier(future.astype(jnp.bfloat16)).astype(jnp.float32)
        log_gaps = cumul[:, :, :, None] - cumul[:, :, None, :]
        rows_idx = lax.broadcasted_iota(jnp.int32, (TOK_DEV, TOK_DEV), 0)
        cols_idx = lax.broadcasted_iota(jnp.int32, (TOK_DEV, TOK_DEV), 1)
        lower_mask = rows_idx >= cols_idx
        mask_decay = jnp.where(lower_mask, jnp.exp(jnp.where(lower_mask, log_gaps, 0.0)), 0.0)
        weights_p = jnp.einsum("nthe,nshe->nhts", grad_attn, value_f) * mask_decay
        weights_p = lax.optimization_barrier(weights_p.astype(jnp.bfloat16)).astype(jnp.float32)
        weights_a = jnp.einsum("nthd,nshd->nhts", query_f, key_f) * mask_decay
        weights_a = lax.optimization_barrier(weights_a.astype(jnp.bfloat16)).astype(jnp.float32)
        state_f = saved_state.astype(jnp.float32)
        after = jnp.exp(cumul[:, :, -1:] - cumul).transpose(0, 2, 1)[..., None]
        grad_q = jnp.einsum("nhts,nshd->nthd", weights_p, key_f) + growth * jnp.einsum("nthe,nhde->nthd", grad_attn, state_f)
        grad_k = jnp.einsum("nhts,nthd->nshd", weights_p, query_f) + after * jnp.einsum("nshe,nhde->nshd", value_f, future_f)
        grad_v = jnp.einsum("nhts,nthe->nshe", weights_a, grad_attn) + after * jnp.einsum("nshd,nhde->nshe", key_f, future_f)
        return (grad_q.reshape(SPAN_OF_STEPS, HD).astype(jnp.bfloat16),
                grad_k.reshape(SPAN_OF_STEPS, HD).astype(jnp.bfloat16),
                grad_v.reshape(SPAN_OF_STEPS, HD).astype(jnp.bfloat16))

    grad_q, grad_k, grad_v = lax.map(one_sequence, (grad_out, queries, keys_in, values, log_decay, kv_state))
    return (grad_q, grad_k, grad_v)
```

```python
import jax
import jax.numpy as jnp
from jax import lax
from jax.sharding import PartitionSpec as P

RADIX = 4


def shifted(array, axis, size, distance):
    pairs = [(src, src - distance) for src in range(distance, size)]
    return lax.ppermute(array, axis, pairs)


def compose(earlier, later, width):
    grow = earlier[:, width:width + 1]
    return jnp.concatenate(
        [earlier[:, :width] + grow * later[:, :width], earlier[:, width:] * later[:, width:]],
        axis=1,
    )


def entering_after(packed, axis, width):
    size = lax.axis_size(axis)
    parts = [shifted(packed, axis, size, k) for k in range(1, RADIX + 1)]
    state = parts[-1]
    for part in reversed(parts[:-1]):
        state = compose(part, state, width)
    span = RADIX
    while span < size:
        parts = [shifted(state, axis, size, k * span) for k in range(1, RADIX)]
        tail = parts[-1]
        for part in reversed(parts[:-1]):
            tail = compose(part, tail, width)
        state = compose(state, tail, width)
        span *= RADIX
    return state


def on_device(grad_out, w_out, queries, keys_in, values, log_decay, kv_state):
    token_rows = grad_out[0]
    length_dev = token_rows.shape[0]
    head_count = log_decay.shape[1]
    head_size = queries.shape[2] // head_count
    projected = lax.dot_general(
        token_rows,
        lax.all_gather(w_out, "dp", axis=1, tiled=True),
        (((1,), (1,)), ((), ())),
        preferred_element_type=jnp.float32,
    )
    grad_attn = projected.astype(jnp.bfloat16).reshape(length_dev, head_count, head_size)
    query_heads = queries[0].reshape(length_dev, head_count, head_size)
    key_heads = keys_in[0].reshape(length_dev, head_count, head_size)
    value_heads = values[0].reshape(length_dev, head_count, head_size)
    cumul = jnp.cumsum(log_decay[0], axis=1)
    block_total = cumul[:, -1]
    growth = jnp.exp(cumul).T[:, :, None]
    scaled_q = (query_heads * growth).astype(jnp.bfloat16)
    block_terms = jnp.einsum(
        "thd,the->hde", scaled_q, grad_attn, preferred_element_type=jnp.float32
    )
    block_decay = jnp.exp(block_total)
    width = head_size * head_size
    packed = jnp.concatenate(
        [
            block_terms.reshape(head_count, width),
            jnp.broadcast_to(block_decay[:, None], (head_count, 128)),
        ],
        axis=1,
    )
    combined = entering_after(packed, "seq", width)
    future_low = combined[:, :width].reshape(head_count, head_size, head_size).astype(jnp.bfloat16)
    log_gaps = cumul[:, :, None] - cumul[:, None, :]
    rows_idx = lax.broadcasted_iota(jnp.int32, (length_dev, length_dev), 0)
    cols_idx = lax.broadcasted_iota(jnp.int32, (length_dev, length_dev), 1)
    lower_mask = rows_idx >= cols_idx
    mask_decay = jnp.where(lower_mask, jnp.exp(jnp.where(lower_mask, log_gaps, 0.0)), 0.0)
    weights_p = (
        jnp.einsum("the,she->hts", grad_attn, value_heads, preferred_element_type=jnp.float32)
        * mask_decay
    ).astype(jnp.bfloat16)
    weights_a = (
        jnp.einsum("thd,shd->hts", query_heads, key_heads, preferred_element_type=jnp.float32)
        * mask_decay
    ).astype(jnp.bfloat16)
    saved_state = kv_state[0, 0]
    after = jnp.exp(block_total[:, None] - cumul).T[:, :, None]
    grad_q = jnp.einsum("hts,shd->thd", weights_p, key_heads, preferred_element_type=jnp.float32)
    grad_q = grad_q + growth * jnp.einsum(
        "the,hde->thd", grad_attn, saved_state, preferred_element_type=jnp.float32
    )
    grad_k = jnp.einsum("hts,thd->shd", weights_p, query_heads, preferred_element_type=jnp.float32)
    grad_k = grad_k + after * jnp.einsum(
        "she,hde->shd", value_heads, future_low, preferred_element_type=jnp.float32
    )
    grad_v = jnp.einsum("hts,the->she", weights_a, grad_attn, preferred_element_type=jnp.float32)
    grad_v = grad_v + after * jnp.einsum(
        "shd,hde->she", key_heads, future_low, preferred_element_type=jnp.float32
    )
    out_shape = (1, length_dev, head_count * head_size)
    return (
        grad_q.reshape(out_shape).astype(jnp.bfloat16),
        grad_k.reshape(out_shape).astype(jnp.bfloat16),
        grad_v.reshape(out_shape).astype(jnp.bfloat16),
    )


def solution(mesh):
    return jax.shard_map(
        on_device,
        mesh=mesh,
        in_specs=(
            P("dp", "seq", None),
            P(None, "dp"),
            P("dp", "seq", None),
            P("dp", "seq", None),
            P("dp", "seq", None),
            P("dp", None, "seq"),
            P("dp", "seq", None, None, None),
        ),
        out_specs=(P("dp", "seq", None), P("dp", "seq", None), P("dp", "seq", None)),
        check_vma=False,
    )
```

```python
import jax
import jax.numpy as jnp
from jax import lax
from jax.sharding import PartitionSpec as P

RADIX = 4


def shifted(array, axis, size, distance):
    pairs = [(src, src - distance) for src in range(distance, size)]
    return lax.ppermute(array, axis, pairs)


def compose(earlier, later, width):
    grow = earlier[:, width:width + 1]
    return jnp.concatenate(
        [earlier[:, :width] + grow * later[:, :width], earlier[:, width:] * later[:, width:]],
        axis=1,
    )


def entering_after(packed, axis, width):
    size = lax.axis_size(axis)
    parts = [shifted(packed, axis, size, k) for k in range(1, RADIX + 1)]
    state = parts[-1]
    for part in reversed(parts[:-1]):
        state = compose(part, state, width)
    span = RADIX
    while span < size:
        parts = [shifted(state, axis, size, k * span) for k in range(1, RADIX)]
        tail = parts[-1]
        for part in reversed(parts[:-1]):
            tail = compose(part, tail, width)
        state = compose(state, tail, width)
        span *= RADIX
    return state


def entering_by_transpose(block_terms, block_total, axis):
    size = lax.axis_size(axis)
    heads, rows, cols = block_terms.shape
    piece = heads * rows * cols // size
    owner_head = (jnp.arange(size) * piece) // (rows * cols)
    payload = jnp.concatenate(
        [block_terms.reshape(size, piece), block_total[owner_head][:, None]], axis=1
    )
    gathered = lax.all_to_all(payload, axis, 0, 0, tiled=True)
    totals = gathered[:, piece]
    later = lax.broadcasted_iota(jnp.int32, (size, size), 1) > lax.broadcasted_iota(
        jnp.int32, (size, size), 0
    )
    between = jnp.dot(
        jnp.where(later, totals[None, :], 0.0),
        later.astype(jnp.float32),
        precision=lax.Precision.HIGHEST,
    )
    weights = jnp.where(later, jnp.exp(jnp.where(later, between, 0.0)), 0.0)
    folded = jnp.dot(weights, gathered[:, :piece], precision=lax.Precision.HIGHEST)
    returned = lax.all_to_all(folded, axis, 0, 0, tiled=True)
    return returned.reshape(heads, rows, cols)


Z_HI = 2
X_SIZE = 8
Y_SIZE = 8
CORES = 2


def linear(z, x, y, core, z_lo_size):
    seq = ((x * Z_HI + z // z_lo_size) * Y_SIZE + y) * CORES + core
    return (z % z_lo_size) * (X_SIZE * Z_HI * Y_SIZE * CORES) + seq


def from_offset(array, distance, z_lo_size):
    z_size = z_lo_size * Z_HI
    pairs = []
    for z in range(z_size):
        for x in range(X_SIZE):
            for y in range(Y_SIZE):
                for core in range(CORES):
                    src = linear((z + distance) % z_size, x, y, core, z_lo_size)
                    pairs.append((src, linear(z, x, y, core, z_lo_size)))
    return lax.ppermute(array, ("dp", "seq"), pairs)


def partial_product(token_rows, block, index, cols):
    rows = lax.dynamic_slice_in_dim(token_rows, index * cols, cols, axis=1)
    return lax.dot_general(rows, block, (((1,), (1,)), ((), ())), preferred_element_type=jnp.float32)


def project(token_rows, w_local):
    z_lo_size = lax.axis_size("dp")
    z_lo = lax.axis_index("dp")
    core = lax.axis_index("seq") % CORES
    cols = w_local.shape[1]
    half = w_local.shape[0] // CORES
    quarter = half // 2
    mine = lax.dynamic_slice_in_dim(w_local, core * half, half, 0)
    theirs = lax.dynamic_slice_in_dim(w_local, (1 - core) * half, half, 0)
    near_up = from_offset(mine, 1, z_lo_size)
    near_down = from_offset(mine, -1, z_lo_size)
    far = jnp.concatenate(
        [
            from_offset(mine[:quarter], 2, z_lo_size),
            from_offset(mine[quarter:], -2, z_lo_size),
        ],
        axis=0,
    )
    fetched = [near_up, near_down, far]
    offsets = [1, z_lo_size - 1, 2]
    swapped = lax.ppermute(
        jnp.stack(fetched), "seq",
        [(i, i ^ 1) for i in range(lax.axis_size("seq"))],
    )
    own_mine = partial_product(token_rows, mine, z_lo, cols)
    own_theirs = partial_product(token_rows, theirs, z_lo, cols)
    for k in range(3):
        index = (z_lo + offsets[k]) % z_lo_size
        own_mine = own_mine + partial_product(token_rows, fetched[k], index, cols)
        own_theirs = own_theirs + partial_product(token_rows, swapped[k], index, cols)
    return jnp.where(
        core == 0,
        jnp.concatenate([own_mine, own_theirs], axis=1),
        jnp.concatenate([own_theirs, own_mine], axis=1),
    )


def on_device(grad_out, w_out, queries, keys_in, values, log_decay, kv_state):
    token_rows = grad_out[0]
    length_dev = token_rows.shape[0]
    head_count = log_decay.shape[1]
    head_size = queries.shape[2] // head_count
    projected = project(token_rows, w_out)
    grad_attn = projected.astype(jnp.bfloat16).reshape(length_dev, head_count, head_size)
    query_heads = queries[0].reshape(length_dev, head_count, head_size)
    key_heads = keys_in[0].reshape(length_dev, head_count, head_size)
    value_heads = values[0].reshape(length_dev, head_count, head_size)
    cumul = jnp.cumsum(log_decay[0], axis=1)
    block_total = cumul[:, -1]
    growth = jnp.exp(cumul).T[:, :, None]
    scaled_q = (query_heads * growth).astype(jnp.bfloat16)
    block_terms = jnp.einsum(
        "thd,the->hde", scaled_q, grad_attn, preferred_element_type=jnp.float32
    )
    block_decay = jnp.exp(block_total)
    width = head_size * head_size
    packed = jnp.concatenate(
        [
            block_terms.reshape(head_count, width),
            jnp.broadcast_to(block_decay[:, None], (head_count, 128)),
        ],
        axis=1,
    )
    future = entering_by_transpose(block_terms, block_total, "seq")
    future_low = future.astype(jnp.bfloat16)
    log_gaps = cumul[:, :, None] - cumul[:, None, :]
    rows_idx = lax.broadcasted_iota(jnp.int32, (length_dev, length_dev), 0)
    cols_idx = lax.broadcasted_iota(jnp.int32, (length_dev, length_dev), 1)
    lower_mask = rows_idx >= cols_idx
    mask_decay = jnp.where(lower_mask, jnp.exp(jnp.where(lower_mask, log_gaps, 0.0)), 0.0)
    weights_p = (
        jnp.einsum("the,she->hts", grad_attn, value_heads, preferred_element_type=jnp.float32)
        * mask_decay
    ).astype(jnp.bfloat16)
    weights_a = (
        jnp.einsum("thd,shd->hts", query_heads, key_heads, preferred_element_type=jnp.float32)
        * mask_decay
    ).astype(jnp.bfloat16)
    saved_state = kv_state[0, 0]
    after = jnp.exp(block_total[:, None] - cumul).T[:, :, None]
    grad_q = jnp.einsum("hts,shd->thd", weights_p, key_heads, preferred_element_type=jnp.float32)
    grad_q = grad_q + growth * jnp.einsum(
        "the,hde->thd", grad_attn, saved_state, preferred_element_type=jnp.float32
    )
    grad_k = jnp.einsum("hts,thd->shd", weights_p, query_heads, preferred_element_type=jnp.float32)
    grad_k = grad_k + after * jnp.einsum(
        "she,hde->shd", value_heads, future_low, preferred_element_type=jnp.float32
    )
    grad_v = jnp.einsum("hts,the->she", weights_a, grad_attn, preferred_element_type=jnp.float32)
    grad_v = grad_v + after * jnp.einsum(
        "shd,hde->she", key_heads, future_low, preferred_element_type=jnp.float32
    )
    out_shape = (1, length_dev, head_count * head_size)
    return (
        grad_q.reshape(out_shape).astype(jnp.bfloat16),
        grad_k.reshape(out_shape).astype(jnp.bfloat16),
        grad_v.reshape(out_shape).astype(jnp.bfloat16),
    )


def solution(mesh):
    return jax.shard_map(
        on_device,
        mesh=mesh,
        in_specs=(
            P("dp", "seq", None),
            P(None, "dp"),
            P("dp", "seq", None),
            P("dp", "seq", None),
            P("dp", "seq", None),
            P("dp", None, "seq"),
            P("dp", "seq", None, None, None),
        ),
        out_specs=(P("dp", "seq", None), P("dp", "seq", None), P("dp", "seq", None)),
        check_vma=False,
    )
```

```python
import jax
import jax.numpy as jnp
from jax import lax
from jax.sharding import PartitionSpec as P

RADIX = 4


def shifted(array, axis, size, distance):
    pairs = [(src, src - distance) for src in range(distance, size)]
    return lax.ppermute(array, axis, pairs)


def compose(earlier, later, width):
    grow = earlier[:, width:width + 1]
    return jnp.concatenate(
        [earlier[:, :width] + grow * later[:, :width], earlier[:, width:] * later[:, width:]],
        axis=1,
    )


def entering_after(packed, axis, width):
    size = lax.axis_size(axis)
    parts = [shifted(packed, axis, size, k) for k in range(1, RADIX + 1)]
    state = parts[-1]
    for part in reversed(parts[:-1]):
        state = compose(part, state, width)
    span = RADIX
    while span < size:
        parts = [shifted(state, axis, size, k * span) for k in range(1, RADIX)]
        tail = parts[-1]
        for part in reversed(parts[:-1]):
            tail = compose(part, tail, width)
        state = compose(state, tail, width)
        span *= RADIX
    return state


def gather_groups(message, outer):
    return lax.all_to_all(jnp.broadcast_to(message, (outer,) + message.shape), "sx", 0, 0, tiled=True)


def exact_weights(logs, start):
    count = logs.shape[0]
    rows = start.shape[0]
    index = lax.broadcasted_iota(jnp.int32, (rows, count), 1)
    later = index > start[:, None]
    upper = lax.broadcasted_iota(jnp.int32, (count, count), 0) < lax.broadcasted_iota(
        jnp.int32, (count, count), 1
    )
    chosen = jnp.where(later, logs[None, :], 0.0)
    between = jnp.dot(chosen, upper.astype(jnp.float32), precision=lax.Precision.HIGHEST)
    weights = jnp.where(later, jnp.exp(jnp.where(later, between, 0.0)), 0.0)
    return weights, jnp.sum(chosen, axis=1)


def entering_two_level(block_terms, block_total):
    inner = lax.axis_size("sy")
    heads, rows, cols = block_terms.shape
    piece = heads * rows * cols // inner
    owner_head = (jnp.arange(inner) * piece) // (rows * cols)
    payload = jnp.concatenate(
        [block_terms.reshape(inner, piece), block_total[owner_head][:, None]], axis=1
    )
    got = lax.all_to_all(payload, "sy", 0, 0, tiled=True)
    weights, tail_log = exact_weights(got[:, piece], jnp.arange(-1, inner))
    folded = jnp.dot(weights, got[:, :piece], precision=lax.Precision.HIGHEST)
    message = jnp.concatenate([folded[0], jnp.broadcast_to(tail_log[0], (128,))])
    outer = lax.axis_size("sx")
    groups = gather_groups(message, outer)
    group_weights, _ = exact_weights(groups[:, piece], lax.axis_index("sx")[None])
    incoming = jnp.dot(group_weights, groups[:, :piece], precision=lax.Precision.HIGHEST)
    future = folded[1:] + jnp.exp(tail_log[1:])[:, None] * incoming
    returned = lax.all_to_all(future, "sy", 0, 0, tiled=True)
    return returned.reshape(heads, rows, cols)


Z_HI = 2
X_SIZE = 8
Y_SIZE = 8
CORES = 2


def linear(z, x, y, core, z_lo_size):
    seq = ((x * Z_HI + z // z_lo_size) * Y_SIZE + y) * CORES + core
    return (z % z_lo_size) * (X_SIZE * Z_HI * Y_SIZE * CORES) + seq


def from_offset(array, distance, z_lo_size):
    z_size = z_lo_size * Z_HI
    pairs = []
    for z in range(z_size):
        for x in range(X_SIZE):
            for y in range(Y_SIZE):
                for core in range(CORES):
                    src = linear((z + distance) % z_size, x, y, core, z_lo_size)
                    pairs.append((src, linear(z, x, y, core, z_lo_size)))
    return lax.ppermute(array, ("dp", "sx", "sy"), pairs)


def partial_product(token_rows, block, index, cols):
    rows = lax.dynamic_slice_in_dim(token_rows, index * cols, cols, axis=1)
    return lax.dot_general(rows, block, (((1,), (1,)), ((), ())), preferred_element_type=jnp.float32)


def project(token_rows, w_local):
    z_lo_size = lax.axis_size("dp")
    z_lo = lax.axis_index("dp")
    core = lax.axis_index("sy") % CORES
    cols = w_local.shape[1]
    half = w_local.shape[0] // CORES
    quarter = half // 2
    mine = lax.dynamic_slice_in_dim(w_local, core * half, half, 0)
    theirs = lax.dynamic_slice_in_dim(w_local, (1 - core) * half, half, 0)
    near_up = from_offset(mine, 1, z_lo_size)
    near_down = from_offset(mine, -1, z_lo_size)
    far = jnp.concatenate(
        [
            from_offset(mine[:quarter], 2, z_lo_size),
            from_offset(mine[quarter:], -2, z_lo_size),
        ],
        axis=0,
    )
    fetched = [near_up, near_down, far]
    offsets = [1, z_lo_size - 1, 2]
    swapped = lax.ppermute(
        jnp.stack(fetched), "sy",
        [(i, i ^ 1) for i in range(lax.axis_size("sy"))],
    )
    own_mine = partial_product(token_rows, mine, z_lo, cols)
    own_theirs = partial_product(token_rows, theirs, z_lo, cols)
    for k in range(3):
        index = (z_lo + offsets[k]) % z_lo_size
        own_mine = own_mine + partial_product(token_rows, fetched[k], index, cols)
        own_theirs = own_theirs + partial_product(token_rows, swapped[k], index, cols)
    return jnp.where(
        core == 0,
        jnp.concatenate([own_mine, own_theirs], axis=1),
        jnp.concatenate([own_theirs, own_mine], axis=1),
    )


def on_device(grad_out, w_out, queries, keys_in, values, log_decay, kv_state):
    token_rows = grad_out[0]
    length_dev = token_rows.shape[0]
    head_count = log_decay.shape[1]
    head_size = queries.shape[2] // head_count
    projected = project(token_rows, w_out)
    grad_attn = projected.astype(jnp.bfloat16).reshape(length_dev, head_count, head_size)
    query_heads = queries[0].reshape(length_dev, head_count, head_size)
    key_heads = keys_in[0].reshape(length_dev, head_count, head_size)
    value_heads = values[0].reshape(length_dev, head_count, head_size)
    cumul = jnp.cumsum(log_decay[0], axis=1)
    block_total = cumul[:, -1]
    growth = jnp.exp(cumul).T[:, :, None]
    scaled_q = (query_heads * growth).astype(jnp.bfloat16)
    block_terms = jnp.einsum(
        "thd,the->hde", scaled_q, grad_attn, preferred_element_type=jnp.float32
    )
    block_decay = jnp.exp(block_total)
    width = head_size * head_size
    packed = jnp.concatenate(
        [
            block_terms.reshape(head_count, width),
            jnp.broadcast_to(block_decay[:, None], (head_count, 128)),
        ],
        axis=1,
    )
    future = entering_two_level(block_terms, block_total)
    future_low = future.astype(jnp.bfloat16)
    log_gaps = cumul[:, :, None] - cumul[:, None, :]
    rows_idx = lax.broadcasted_iota(jnp.int32, (length_dev, length_dev), 0)
    cols_idx = lax.broadcasted_iota(jnp.int32, (length_dev, length_dev), 1)
    lower_mask = rows_idx >= cols_idx
    mask_decay = jnp.where(lower_mask, jnp.exp(jnp.where(lower_mask, log_gaps, 0.0)), 0.0)
    weights_p = (
        jnp.einsum("the,she->hts", grad_attn, value_heads, preferred_element_type=jnp.float32)
        * mask_decay
    ).astype(jnp.bfloat16)
    weights_a = (
        jnp.einsum("thd,shd->hts", query_heads, key_heads, preferred_element_type=jnp.float32)
        * mask_decay
    ).astype(jnp.bfloat16)
    saved_state = kv_state[0, 0]
    after = jnp.exp(block_total[:, None] - cumul).T[:, :, None]
    grad_q = jnp.einsum("hts,shd->thd", weights_p, key_heads, preferred_element_type=jnp.float32)
    grad_q = grad_q + growth * jnp.einsum(
        "the,hde->thd", grad_attn, saved_state, preferred_element_type=jnp.float32
    )
    grad_k = jnp.einsum("hts,thd->shd", weights_p, query_heads, preferred_element_type=jnp.float32)
    grad_k = grad_k + after * jnp.einsum(
        "she,hde->shd", value_heads, future_low, preferred_element_type=jnp.float32
    )
    grad_v = jnp.einsum("hts,the->she", weights_a, grad_attn, preferred_element_type=jnp.float32)
    grad_v = grad_v + after * jnp.einsum(
        "shd,hde->she", key_heads, future_low, preferred_element_type=jnp.float32
    )
    out_shape = (1, length_dev, head_count * head_size)
    return (
        grad_q.reshape(out_shape).astype(jnp.bfloat16),
        grad_k.reshape(out_shape).astype(jnp.bfloat16),
        grad_v.reshape(out_shape).astype(jnp.bfloat16),
    )


def solution(mesh):
    inner = Y_SIZE * CORES
    blocks = mesh.devices.reshape(mesh.shape["dp"], mesh.shape["seq"] // inner, inner)
    grid = jax.sharding.Mesh(blocks, ("dp", "sx", "sy"))
    seq = ("sx", "sy")
    return jax.shard_map(
        on_device,
        mesh=grid,
        in_specs=(
            P("dp", seq, None),
            P(None, "dp"),
            P("dp", seq, None),
            P("dp", seq, None),
            P("dp", seq, None),
            P("dp", None, seq),
            P("dp", seq, None, None, None),
        ),
        out_specs=(P("dp", seq, None), P("dp", seq, None), P("dp", seq, None)),
        check_vma=False,
    )
```

```python
import jax
import jax.numpy as jnp
from jax import lax
from jax.sharding import PartitionSpec as P

RADIX = 4


def shifted(array, axis, size, distance):
    pairs = [(src, src - distance) for src in range(distance, size)]
    return lax.ppermute(array, axis, pairs)


def compose(earlier, later, width):
    grow = earlier[:, width:width + 1]
    return jnp.concatenate(
        [earlier[:, :width] + grow * later[:, :width], earlier[:, width:] * later[:, width:]],
        axis=1,
    )


def entering_after(packed, axis, width):
    size = lax.axis_size(axis)
    parts = [shifted(packed, axis, size, k) for k in range(1, RADIX + 1)]
    state = parts[-1]
    for part in reversed(parts[:-1]):
        state = compose(part, state, width)
    span = RADIX
    while span < size:
        parts = [shifted(state, axis, size, k * span) for k in range(1, RADIX)]
        tail = parts[-1]
        for part in reversed(parts[:-1]):
            tail = compose(part, tail, width)
        state = compose(state, tail, width)
        span *= RADIX
    return state


def exact_weights(logs, start):
    count = logs.shape[0]
    rows = start.shape[0]
    index = lax.broadcasted_iota(jnp.int32, (rows, count), 1)
    later = index > start[:, None]
    upper = lax.broadcasted_iota(jnp.int32, (count, count), 0) < lax.broadcasted_iota(
        jnp.int32, (count, count), 1
    )
    chosen = jnp.where(later, logs[None, :], 0.0)
    between = jnp.dot(chosen, upper.astype(jnp.float32), precision=lax.Precision.HIGHEST)
    weights = jnp.where(later, jnp.exp(jnp.where(later, between, 0.0)), 0.0)
    return weights, jnp.sum(chosen, axis=1)


def tiles(rows, scalar, height):
    count = rows.shape[0]
    body = rows.reshape(count, -1, 128)
    spare = height - body.shape[1] - 1
    return jnp.concatenate(
        [
            body,
            jnp.broadcast_to(scalar[:, None, None], (count, 1, 128)),
            jnp.zeros((count, spare, 128), rows.dtype),
        ],
        axis=1,
    )


def entering_two_level(block_terms, block_total):
    inner = lax.axis_size("sy")
    heads, rows, cols = block_terms.shape
    piece = heads * rows * cols // inner
    height = piece // 128 + 1
    height = -(-height // 8) * 8
    owner_head = (jnp.arange(inner) * piece) // (rows * cols)
    payload = tiles(block_terms.reshape(inner, piece), block_total[owner_head], height)
    got = lax.all_to_all(payload, "sy", 0, 0, tiled=True)
    weights, tail_log = exact_weights(got[:, piece // 128, 0], jnp.arange(-1, inner))
    terms = got[:, : piece // 128].reshape(inner, piece)
    folded = jnp.dot(weights, terms, precision=lax.Precision.HIGHEST)
    outer = lax.axis_size("sx")
    message = tiles(folded[:1], tail_log[:1], height)
    groups = lax.all_to_all(
        jnp.broadcast_to(message, (outer,) + message.shape[1:]), "sx", 0, 0, tiled=True
    )
    group_weights, _ = exact_weights(groups[:, piece // 128, 0], lax.axis_index("sx")[None])
    incoming = jnp.dot(
        group_weights, groups[:, : piece // 128].reshape(outer, piece),
        precision=lax.Precision.HIGHEST,
    )
    future = folded[1:] + jnp.exp(tail_log[1:])[:, None] * incoming
    returned = lax.all_to_all(future.reshape(inner, -1, 128), "sy", 0, 0, tiled=True)
    return returned.reshape(heads, rows, cols)


Z_HI = 2
X_SIZE = 8
Y_SIZE = 8
CORES = 2


def linear(z, x, y, core, z_lo_size):
    seq = ((x * Z_HI + z // z_lo_size) * Y_SIZE + y) * CORES + core
    return (z % z_lo_size) * (X_SIZE * Z_HI * Y_SIZE * CORES) + seq


def from_offset(array, distances, z_lo_size):
    z_size = z_lo_size * Z_HI
    pairs = []
    for z in range(z_size):
        for x in range(X_SIZE):
            for y in range(Y_SIZE):
                for core in range(CORES):
                    src = linear((z + distances[core]) % z_size, x, y, core, z_lo_size)
                    pairs.append((src, linear(z, x, y, core, z_lo_size)))
    return lax.ppermute(array, ("dp", "sx", "sy"), pairs)


def partial_product(token_rows, block, index, cols):
    rows = lax.dynamic_slice_in_dim(token_rows, index * cols, cols, axis=1)
    return lax.dot_general(rows, block, (((1,), (1,)), ((), ())), preferred_element_type=jnp.float32)


def project(token_rows, w_local):
    z_lo_size = lax.axis_size("dp")
    z_lo = lax.axis_index("dp")
    core = lax.axis_index("sy") % CORES
    cols = w_local.shape[1]
    half = w_local.shape[0] // CORES
    near = from_offset(w_local, (1, -1), z_lo_size)
    far = from_offset(lax.dynamic_slice_in_dim(w_local, core * half, half, 0), (2, -2), z_lo_size)
    swapped = lax.ppermute(
        jnp.concatenate([near, far], axis=0), "sy",
        [(i, i ^ 1) for i in range(lax.axis_size("sy"))],
    )
    step = 1 - 2 * core
    total = partial_product(token_rows, w_local, z_lo, cols)
    total = total + partial_product(token_rows, near, (z_lo + step) % z_lo_size, cols)
    total = total + partial_product(
        token_rows, swapped[: w_local.shape[0]], (z_lo - step) % z_lo_size, cols
    )
    far_index = (z_lo + 2) % z_lo_size
    far_mine = partial_product(token_rows, far, far_index, cols)
    far_theirs = partial_product(token_rows, swapped[w_local.shape[0]:], far_index, cols)
    return total + jnp.where(
        core == 0,
        jnp.concatenate([far_mine, far_theirs], axis=1),
        jnp.concatenate([far_theirs, far_mine], axis=1),
    )


def on_device(grad_out, w_out, queries, keys_in, values, log_decay, kv_state):
    token_rows = grad_out[0]
    length_dev = token_rows.shape[0]
    head_count = log_decay.shape[1]
    head_size = queries.shape[2] // head_count
    projected = project(token_rows, w_out)
    grad_attn = projected.astype(jnp.bfloat16).reshape(length_dev, head_count, head_size)
    query_heads = queries[0].reshape(length_dev, head_count, head_size)
    key_heads = keys_in[0].reshape(length_dev, head_count, head_size)
    value_heads = values[0].reshape(length_dev, head_count, head_size)
    cumul = jnp.cumsum(log_decay[0], axis=1)
    block_total = cumul[:, -1]
    growth = jnp.exp(cumul).T[:, :, None]
    scaled_q = (query_heads * growth).astype(jnp.bfloat16)
    block_terms = jnp.einsum(
        "thd,the->hde", scaled_q, grad_attn, preferred_element_type=jnp.float32
    )
    block_decay = jnp.exp(block_total)
    width = head_size * head_size
    packed = jnp.concatenate(
        [
            block_terms.reshape(head_count, width),
            jnp.broadcast_to(block_decay[:, None], (head_count, 128)),
        ],
        axis=1,
    )
    future = entering_two_level(block_terms, block_total)
    future_low = future.astype(jnp.bfloat16)
    log_gaps = cumul[:, :, None] - cumul[:, None, :]
    rows_idx = lax.broadcasted_iota(jnp.int32, (length_dev, length_dev), 0)
    cols_idx = lax.broadcasted_iota(jnp.int32, (length_dev, length_dev), 1)
    lower_mask = rows_idx >= cols_idx
    mask_decay = jnp.where(lower_mask, jnp.exp(jnp.where(lower_mask, log_gaps, 0.0)), 0.0)
    weights_p = (
        jnp.einsum("the,she->hts", grad_attn, value_heads, preferred_element_type=jnp.float32)
        * mask_decay
    ).astype(jnp.bfloat16)
    weights_a = (
        jnp.einsum("thd,shd->hts", query_heads, key_heads, preferred_element_type=jnp.float32)
        * mask_decay
    ).astype(jnp.bfloat16)
    saved_state = kv_state[0, 0]
    after = jnp.exp(block_total[:, None] - cumul).T[:, :, None]
    grad_q = jnp.einsum("hts,shd->thd", weights_p, key_heads, preferred_element_type=jnp.float32)
    grad_q = grad_q + growth * jnp.einsum(
        "the,hde->thd", grad_attn, saved_state, preferred_element_type=jnp.float32
    )
    grad_k = jnp.einsum("hts,thd->shd", weights_p, query_heads, preferred_element_type=jnp.float32)
    grad_k = grad_k + after * jnp.einsum(
        "she,hde->shd", value_heads, future_low, preferred_element_type=jnp.float32
    )
    grad_v = jnp.einsum("hts,the->she", weights_a, grad_attn, preferred_element_type=jnp.float32)
    grad_v = grad_v + after * jnp.einsum(
        "shd,hde->she", key_heads, future_low, preferred_element_type=jnp.float32
    )
    out_shape = (1, length_dev, head_count * head_size)
    return (
        grad_q.reshape(out_shape).astype(jnp.bfloat16),
        grad_k.reshape(out_shape).astype(jnp.bfloat16),
        grad_v.reshape(out_shape).astype(jnp.bfloat16),
    )


def solution(mesh):
    inner = Y_SIZE * CORES
    blocks = mesh.devices.reshape(mesh.shape["dp"], mesh.shape["seq"] // inner, inner)
    grid = jax.sharding.Mesh(blocks, ("dp", "sx", "sy"))
    seq = ("sx", "sy")
    return jax.shard_map(
        on_device,
        mesh=grid,
        in_specs=(
            P("dp", seq, None),
            P(None, "dp"),
            P("dp", seq, None),
            P("dp", seq, None),
            P("dp", seq, None),
            P("dp", None, seq),
            P("dp", seq, None, None, None),
        ),
        out_specs=(P("dp", seq, None), P("dp", seq, None), P("dp", seq, None)),
        check_vma=False,
    )
```
